768 devices in a mesh: ctx: 32 (over y, z_hi), tp: 24 (over z_lo, x, core).
Axes of the slice: x: 4, y: 8, z: 12 (z_hi: 4, z_lo: 3; z = z_hi * 3 + z_lo), core: 2. Of those that a mesh axis runs over, the one named last changes fastest.
Arguments:
- tokens: bfloat16 [16384, 5376], P('ctx'), may hold values from -36 to 36, as said below
- norm_gain: float32 [5376], replicated, may hold values from 0.5 to 1.5
- query_weight: bfloat16 [5376, 3072], P(None, 'tp'), may hold values from -0.078125 to 0.078125
- keyval_weight: bfloat16 [5376, 3072], P(None, 'tp'), may hold values from -0.07637626 to 0.07637626
- query_gain: float32 [128], replicated, may hold values from 0.5 to 40
- key_gain: float32 [128], replicated, may hold values from 0.5 to 40
- out_weight: bfloat16 [3072, 5376], P('tp'), may hold values from -2.8 to 2.8
- post_gain: float32 [5376], P('tp'), may hold values from 0.5 to 1.5
Outputs:
- layer_out: bfloat16 [16384, 5376], P('ctx', 'tp')
The draws below stay inside these ranges and needn't reach their ends.
Inputs may be any that keep to these rules, and one draw needn't show every extreme that they name: `tokens`: each row and feature has its own scale.
All inputs are finite; a program needn't handle non-finite values.
Results may differ from the reference program's by a relative error of at most 0.03.
Values may be sent and summed in bfloat16 or wider, within the bound.
No kernel may reach another device: no remote copies, remote signals or barrier semaphores. Data moves between devices by JAX's collectives and lax.ppermute only.
A program may use at most 128 MiB of HBM per device.

```python
import math
import jax
import jax.numpy as jnp
from jax import lax

D = 5376
HD = 128
WIN = 1024
TOK_DEV = 512
TOKENS = 16384
HQ = 24
KVH = 12
N_CTX = 32


def draw_tokens(key, part):
    subkeys = jax.random.split(key, 3)
    row_scale = jnp.exp(jax.random.uniform(subkeys[0], (TOKENS, 1), jnp.float32, math.log(0.3), math.log(3.0)))
    col_scale = jnp.exp(jax.random.uniform(subkeys[1], (1, D), jnp.float32, math.log(0.5), math.log(2.0)))
    base_values = jax.random.normal(subkeys[2], (TOKENS, D), jnp.float32)
    base_values = jnp.clip(base_values, -6.0, 6.0)
    return (base_values * row_scale * col_scale).astype(jnp.bfloat16)


def draw_keyval_weight(key, part):
    subkeys = jax.random.split(jax.random.fold_in(key, 31), 3)
    key_part = jnp.clip(jax.random.normal(subkeys[0], (D, KVH, 1, HD), jnp.float32), -4.0, 4.0)
    own_part = jnp.clip(jax.random.normal(subkeys[1], (D, KVH, 1, HD), jnp.float32), -4.0, 4.0)
    shared_part = jnp.clip(jax.random.normal(subkeys[2], (D, 1, 1, HD), jnp.float32), -4.0, 4.0)
    value_part = 0.8 * shared_part + 0.6 * own_part
    joined = jnp.concatenate([key_part, value_part], axis=2) * D ** (-0.5)
    return joined.reshape(D, KVH * 2 * HD).astype(jnp.bfloat16)


def head_gain(key, salt_value):
    own_key = jax.random.fold_in(key, salt_value)
    subkeys = jax.random.split(own_key, 1)
    return jnp.exp(jax.random.uniform(subkeys[0], (HD,), jnp.float32, math.log(0.5), math.log(2.0)))


def draw_query_gain(key, part):
    return head_gain(key, 21)


def draw_key_gain(key, part):
    return head_gain(key, 22)


def draw_out_weight(key, part):
    subkeys = jax.random.split(jax.random.fold_in(key, 41), 3)
    total_rows = HQ * HD
    columns_frac = jnp.arange(D, dtype=jnp.float32) / D
    spread_scale = jnp.exp(jax.random.uniform(subkeys[0], (1, D), jnp.float32, 0.0, math.log(10.0)))
    rising = 3.0 ** columns_frac
    shared_rows = jnp.clip(jax.random.normal(subkeys[1], (HD, D), jnp.float32), -4.0, 4.0)
    own_rows = jnp.clip(jax.random.normal(subkeys[2], (total_rows, D), jnp.float32), -4.0, 4.0)
    mixed = 0.75 * jnp.tile(shared_rows, (HQ, 1)) + 0.5 * own_rows
    head_of_row = jnp.arange(total_rows, dtype=jnp.int32) // HD
    block_of_col = jnp.arange(D, dtype=jnp.int32) * HQ // D
    far_block = (head_of_row + HQ // 2) % HQ
    boost = jnp.where(head_of_row[:, None] == block_of_col[None, :], 4.0, 1.0)
    boost = jnp.where(far_block[:, None] == block_of_col[None, :], 5.0, boost)
    limit = 2.8
    values = mixed * boost * rising[None, :] * spread_scale * (0.15 * total_rows ** (-0.5))
    return jnp.clip(values, -limit, limit).astype(jnp.bfloat16)


def block_levels(key, dims, cuts, low, top_value):
    def one(position, parts):
        heights = jax.random.uniform(jax.random.fold_in(jax.random.fold_in(key, 6), position), (parts,), jnp.float32, low / len(cuts), top_value / len(cuts))
        return jnp.repeat(jnp.exp(heights), dims[position] // parts).reshape((-1,) + (1,) * (len(dims) - position - 1))

    factor_of = one(*cuts[0])
    for cut in cuts[1:]:
        factor_of = factor_of * one(*cut)
    return factor_of


def centred(key, extent, width, most, shards=(), kind=jnp.bfloat16):
    result = width * jax.random.normal(key, extent, jnp.float32)
    if shards:
        result = result * block_levels(key, extent, shards, -0.22, 0.18)
    return jnp.clip(result, -most, most).astype(kind)


def setup_inputs(seed: int = 0) -> dict:
    seeds = jax.random.split(jax.random.key(seed), 9)
    tokens = draw_tokens(jax.random.fold_in(seeds[8], 71), 0)
    norm_gain = jnp.clip(1.0 + 0.1 * jax.random.normal(seeds[1], (D,), jnp.float32), 0.5, 1.5)
    query_weight = centred(seeds[2], (D, HQ * HD), D ** -0.5, 0.078125, ((1, 24),))
    keyval_weight = draw_keyval_weight(jax.random.fold_in(seeds[8], 71), 0)
    query_gain = draw_query_gain(jax.random.fold_in(seeds[8], 71), 0)
    key_gain = draw_key_gain(jax.random.fold_in(seeds[8], 71), 0)
    out_weight = draw_out_weight(jax.random.fold_in(seeds[8], 71), 0)
    post_gain = jnp.clip(1.0 + 0.1 * jax.random.normal(seeds[7], (D,), jnp.float32), 0.5, 1.5)
    return {"tokens": tokens, "norm_gain": norm_gain, "query_weight": query_weight, "keyval_weight": keyval_weight, "query_gain": query_gain, "key_gain": key_gain, "out_weight": out_weight, "post_gain": post_gain}


epsilon = 1e-06
query_scalar = 168.0
rope_base = 10000.0

def rope_tables(positions, head_width):
    half_width = head_width // 2
    exponent = jnp.arange(half_width, dtype=jnp.float32) * (2.0 / head_width)
    frequency = rope_base ** (-exponent)
    angles = positions.astype(jnp.float32)[:, None] * frequency[None, :]
    cosine = jnp.concatenate([jnp.cos(angles), jnp.cos(angles)], axis=1)
    sine_table = jnp.concatenate([jnp.sin(angles), jnp.sin(angles)], axis=1)
    return (cosine, sine_table)

def rotate(signal, cosine, sine_table):
    half_width = signal.shape[-1] // 2
    turned = jnp.concatenate([-signal[:, half_width:], signal[:, :half_width]], axis=1)
    return signal * cosine + turned * sine_table

def rms_scale(signal, gain_vector):
    return signal * lax.rsqrt(lax.optimization_barrier(jnp.mean(signal * signal, axis=-1, keepdims=True)) + epsilon) * gain_vector

def reference(tokens, norm_gain, query_weight, keyval_weight, query_gain, key_gain, out_weight, post_gain):
    as_float = tokens.astype(jnp.float32)
    normed = rms_scale(as_float, norm_gain).astype(jnp.bfloat16)
    positions = jnp.arange(TOKENS, dtype=jnp.int32)
    cosine, sine_table = rope_tables(positions, HD)
    query_all = jnp.dot(normed, query_weight, preferred_element_type=jnp.float32)
    keyval_all = jnp.dot(normed, keyval_weight, preferred_element_type=jnp.float32)
    window_rows = WIN + TOK_DEV
    padding = jnp.zeros((WIN, HD), jnp.bfloat16)

    def one_head(carried, head_index):
        group_index = head_index // 2
        queries = lax.dynamic_slice_in_dim(query_all, (head_index * HD).astype(jnp.int32), HD, 1)
        queries = (rotate(rms_scale(queries, query_gain), cosine, sine_table) * query_scalar ** (-0.5)).astype(jnp.bfloat16)
        key_rows = lax.dynamic_slice_in_dim(keyval_all, (group_index * 2 * HD).astype(jnp.int32), HD, 1)
        key_rows = rotate(rms_scale(key_rows, key_gain), cosine, sine_table).astype(jnp.bfloat16)
        value_rows = lax.dynamic_slice_in_dim(keyval_all, (group_index * 2 * HD + HD).astype(jnp.int32), HD, 1).astype(jnp.bfloat16)
        key_rows = jnp.concatenate([padding, key_rows], axis=0)
        value_rows = jnp.concatenate([padding, value_rows], axis=0)

        def one_block(block_index):
            first_row = (block_index * TOK_DEV).astype(jnp.int32)
            query_block = lax.dynamic_slice_in_dim(queries, first_row, TOK_DEV, 0)
            key_block = lax.dynamic_slice_in_dim(key_rows, first_row, window_rows, 0)
            value_block = lax.dynamic_slice_in_dim(value_rows, first_row, window_rows, 0)
            scores = jnp.dot(query_block, key_block.T, preferred_element_type=jnp.float32)
            query_pos = first_row + jnp.arange(TOK_DEV, dtype=jnp.int32)
            key_pos = first_row - WIN + jnp.arange(window_rows, dtype=jnp.int32)
            distance = query_pos[:, None] - key_pos[None, :]
            allowed = (key_pos[None, :] >= 0) & (distance >= 0) & (distance < WIN)
            scores = jnp.where(allowed, scores, -1e+30)
            row_max = lax.optimization_barrier(jnp.max(scores, axis=1, keepdims=True))
            lifted = jnp.exp(scores - row_max)
            weights = (lifted / lax.optimization_barrier(jnp.sum(lifted, axis=1, keepdims=True))).astype(jnp.bfloat16)
            return jnp.dot(weights, value_block, preferred_element_type=jnp.float32).astype(jnp.bfloat16)
        attended = lax.map(one_block, jnp.arange(N_CTX, dtype=jnp.int32)).reshape(TOKENS, HD)
        out_rows = lax.dynamic_slice_in_dim(out_weight, (head_index * HD).astype(jnp.int32), HD, 0)
        head_term = jnp.dot(attended, out_rows, preferred_element_type=jnp.float32).astype(jnp.bfloat16)
        head_term = lax.optimization_barrier(head_term)
        return (carried + head_term.astype(jnp.float32), None)
    summed, unused = lax.scan(one_head, jnp.zeros((TOKENS, D), jnp.float32), jnp.arange(HQ, dtype=jnp.int32))
    scaled = rms_scale(summed, post_gain)
    return (as_float + scaled).astype(jnp.bfloat16)
```

```python
import jax
import jax.numpy as jnp
from jax import lax
from jax.sharding import Mesh, PartitionSpec as P

WIN = 1024


epsilon = 1e-06
query_scalar = 168.0
rope_base = 10000.0

TP_AXES = ("zl", "x", "core")


def from_behind(block, axis, distance):
    devices = range(lax.axis_size(axis))
    route = [(i - distance, i) for i in devices if i - distance in devices]
    return lax.ppermute(block, axis, route)


def rope_tables(positions, head_width):
    half_width = head_width // 2
    exponent = jnp.arange(half_width, dtype=jnp.float32) * (2.0 / head_width)
    frequency = rope_base ** (-exponent)
    angles = positions.astype(jnp.float32)[:, None] * frequency[None, :]
    cosine = jnp.concatenate([jnp.cos(angles), jnp.cos(angles)], axis=1)
    sine_table = jnp.concatenate([jnp.sin(angles), jnp.sin(angles)], axis=1)
    return (cosine, sine_table)


def rotate(signal, cosine, sine_table):
    half_width = signal.shape[-1] // 2
    turned = jnp.concatenate([-signal[:, half_width:], signal[:, :half_width]], axis=1)
    return signal * cosine + turned * sine_table


def rms_scale(signal, gain_vector):
    return (
        signal
        * lax.rsqrt(jnp.mean(signal * signal, axis=-1, keepdims=True) + epsilon)
        * gain_vector
    )


def body(
    tokens, norm_gain, query_weight, keyval_weight, query_gain, key_gain, out_weight, post_gain
):
    tok_rows = tokens.shape[0]
    model_width = tokens.shape[1]
    head_width = query_weight.shape[1]
    col_share = post_gain.shape[0]
    n_zl = lax.axis_size("zl")
    n_x = lax.axis_size("x")
    n_core = lax.axis_size("core")
    ctx_index = lax.axis_index("ctx")
    core_index = lax.axis_index("core")
    tp_index = (lax.axis_index("zl") * n_x + lax.axis_index("x")) * n_core + core_index
    is_even = core_index == 0

    as_float = tokens.astype(jnp.float32)
    normed = rms_scale(as_float, norm_gain).astype(jnp.bfloat16)
    positions = ctx_index * tok_rows + jnp.arange(tok_rows, dtype=jnp.int32)
    cosine, sine_table = rope_tables(positions, head_width)

    projected = jnp.dot(normed, keyval_weight, preferred_element_type=jnp.float32)
    rotated = rotate(rms_scale(projected, key_gain), cosine, sine_table)
    own_block = jnp.where(is_even, rotated, projected).astype(jnp.bfloat16)
    span_count = WIN // tok_rows
    earlier = [from_behind(own_block, "ctx", offset) for offset in range(span_count, 0, -1)]
    own_window = jnp.concatenate(earlier + [own_block], axis=0)
    other_window = lax.ppermute(own_window, "core", [(0, 1), (1, 0)])
    key_window = jnp.where(is_even, own_window, other_window)
    value_window = jnp.where(is_even, other_window, own_window)

    queries = jnp.dot(normed, query_weight, preferred_element_type=jnp.float32)
    queries = (
        rotate(rms_scale(queries, query_gain), cosine, sine_table) * query_scalar ** (-0.5)
    ).astype(jnp.bfloat16)

    key_pos = ctx_index * tok_rows - WIN + jnp.arange(WIN + tok_rows, dtype=jnp.int32)
    distance = positions[:, None] - key_pos[None, :]
    allowed = (key_pos[None, :] >= 0) & (distance >= 0) & (distance < WIN)
    scores = lax.dot_general(
        queries,
        key_window,
        (((1,), (1,)), ((), ())),
        preferred_element_type=jnp.float32,
    )
    scores = jnp.where(allowed, scores, -1e30)
    row_max = jnp.max(scores, axis=1, keepdims=True)
    lifted = jnp.exp(scores - row_max)
    weights = (lifted / jnp.sum(lifted, axis=1, keepdims=True)).astype(jnp.bfloat16)
    attended = jnp.dot(weights, value_window, preferred_element_type=jnp.float32).astype(
        jnp.bfloat16
    )

    permuted_weight = (
        out_weight.reshape(head_width, n_zl, n_x, n_core, col_share)
        .transpose(0, 3, 2, 1, 4)
        .reshape(head_width, model_width)
    )
    partial_sum = lax.dot_general(
        permuted_weight,
        attended,
        (((0,), (1,)), ((), ())),
        preferred_element_type=jnp.float32,
    )
    reduced = partial_sum.astype(jnp.bfloat16)
    for axis in ("core", "x", "zl"):
        reduced = lax.psum_scatter(reduced, axis, scatter_dimension=0, tiled=True)
    summed = reduced.astype(jnp.float32).T
    squares = jnp.sum(summed * summed, axis=1)
    for axis in ("core", "x", "zl"):
        squares = lax.psum(squares, axis)
    scaled = summed * lax.rsqrt(squares[:, None] / model_width + epsilon) * post_gain
    residual = lax.dynamic_slice_in_dim(tokens, tp_index * col_share, col_share, 1)
    return (residual.astype(jnp.float32) + scaled).astype(jnp.bfloat16)


def solution(mesh):
    n_ctx, n_tp = mesh.devices.shape
    n_core = 2
    n_x = 4
    n_zl = n_tp // (n_core * n_x)
    fine = Mesh(mesh.devices.reshape(n_ctx, n_zl, n_x, n_core), ("ctx",) + TP_AXES)
    return jax.shard_map(
        body,
        mesh=fine,
        in_specs=(
            P("ctx", None),
            P(),
            P(None, TP_AXES),
            P(None, TP_AXES),
            P(),
            P(),
            P(TP_AXES, None),
            P(TP_AXES),
        ),
        out_specs=P("ctx", TP_AXES),
        check_vma=False,
    )
```

```python
import jax
import jax.numpy as jnp
from jax import lax
from jax.sharding import Mesh, PartitionSpec as P

WIN = 1024


epsilon = 1e-06
query_scalar = 168.0
rope_base = 10000.0

TP_AXES = ("zl", "x", "core")


def from_behind(block, axis, distance):
    devices = range(lax.axis_size(axis))
    route = [(i - distance, i) for i in devices if i - distance in devices]
    return lax.ppermute(block, axis, route)


def rope_tables(positions, head_width):
    half_width = head_width // 2
    exponent = jnp.arange(half_width, dtype=jnp.float32) * (2.0 / head_width)
    frequency = rope_base ** (-exponent)
    angles = positions.astype(jnp.float32)[:, None] * frequency[None, :]
    cosine = jnp.concatenate([jnp.cos(angles), jnp.cos(angles)], axis=1)
    sine_table = jnp.concatenate([jnp.sin(angles), jnp.sin(angles)], axis=1)
    return (cosine, sine_table)


def rotate(signal, cosine, sine_table):
    half_width = signal.shape[-1] // 2
    turned = jnp.concatenate([-signal[:, half_width:], signal[:, :half_width]], axis=1)
    return signal * cosine + turned * sine_table


def rms_scale(signal, gain_vector):
    return (
        signal
        * lax.rsqrt(jnp.mean(signal * signal, axis=-1, keepdims=True) + epsilon)
        * gain_vector
    )


def body(
    tokens, norm_gain, query_weight, keyval_weight, query_gain, key_gain, out_weight, post_gain
):
    tok_rows = tokens.shape[0]
    model_width = tokens.shape[1]
    head_width = query_weight.shape[1]
    col_share = post_gain.shape[0]
    n_zl = lax.axis_size("zl")
    n_x = lax.axis_size("x")
    n_core = lax.axis_size("core")
    ctx_index = lax.axis_index("ctx")
    core_index = lax.axis_index("core")
    tp_index = (lax.axis_index("zl") * n_x + lax.axis_index("x")) * n_core + core_index
    is_even = core_index == 0

    as_float = tokens.astype(jnp.float32)
    normed = rms_scale(as_float, norm_gain).astype(jnp.bfloat16)
    positions = ctx_index * tok_rows + jnp.arange(tok_rows, dtype=jnp.int32)
    cosine, sine_table = rope_tables(positions, head_width)

    projected = jnp.dot(normed, keyval_weight, preferred_element_type=jnp.float32)
    rotated = rotate(rms_scale(projected, key_gain), cosine, sine_table)
    own_block = jnp.where(is_even, rotated, projected).astype(jnp.bfloat16)
    span_count = WIN // tok_rows
    earlier = [from_behind(own_block, "ctx", offset) for offset in range(span_count, 0, -1)]
    own_window = jnp.concatenate(earlier + [own_block], axis=0)
    other_window = lax.ppermute(own_window, "core", [(0, 1), (1, 0)])
    key_window = jnp.where(is_even, own_window, other_window)
    value_window = jnp.where(is_even, other_window, own_window)

    queries = jnp.dot(normed, query_weight, preferred_element_type=jnp.float32)
    queries = (
        rotate(rms_scale(queries, query_gain), cosine, sine_table) * query_scalar ** (-0.5)
    ).astype(jnp.bfloat16)

    key_pos = ctx_index * tok_rows - WIN + jnp.arange(WIN + tok_rows, dtype=jnp.int32)
    distance = positions[:, None] - key_pos[None, :]
    allowed = (key_pos[None, :] >= 0) & (distance >= 0) & (distance < WIN)
    scores = lax.dot_general(
        queries,
        key_window,
        (((1,), (1,)), ((), ())),
        preferred_element_type=jnp.float32,
    )
    scores = jnp.where(allowed, scores, -1e30)
    row_max = jnp.max(scores, axis=1, keepdims=True)
    lifted = jnp.exp(scores - row_max)
    weights = (lifted / jnp.sum(lifted, axis=1, keepdims=True)).astype(jnp.bfloat16)
    attended = jnp.dot(weights, value_window, preferred_element_type=jnp.float32).astype(
        jnp.bfloat16
    )

    partial_sum = jnp.dot(attended, out_weight, preferred_element_type=jnp.float32)
    n_tp = n_zl * n_x * n_core
    pieces = partial_sum.astype(jnp.bfloat16).reshape(tok_rows, n_tp, col_share)
    received = lax.all_to_all(pieces, TP_AXES, 1, 1, tiled=True)
    summed = jnp.sum(received.astype(jnp.float32), axis=1)
    squares = jnp.sum(summed * summed, axis=1)
    for axis in ("core", "x", "zl"):
        squares = lax.psum(squares, axis)
    scaled = summed * lax.rsqrt(squares[:, None] / model_width + epsilon) * post_gain
    residual = lax.dynamic_slice_in_dim(tokens, tp_index * col_share, col_share, 1)
    return (residual.astype(jnp.float32) + scaled).astype(jnp.bfloat16)


def solution(mesh):
    n_ctx, n_tp = mesh.devices.shape
    n_core = 2
    n_x = 4
    n_zl = n_tp // (n_core * n_x)
    fine = Mesh(mesh.devices.reshape(n_ctx, n_zl, n_x, n_core), ("ctx",) + TP_AXES)
    return jax.shard_map(
        body,
        mesh=fine,
        in_specs=(
            P("ctx", None),
            P(),
            P(None, TP_AXES),
            P(None, TP_AXES),
            P(),
            P(),
            P(TP_AXES, None),
            P(TP_AXES),
        ),
        out_specs=P("ctx", TP_AXES),
        check_vma=False,
    )
```

```python
import jax
import jax.numpy as jnp
from jax import lax
from jax.sharding import Mesh, PartitionSpec as P

WIN = 1024


epsilon = 1e-06
query_scalar = 168.0
rope_base = 10000.0

TP_AXES = ("zl", "x", "core")


def from_behind(block, axis, distance):
    devices = range(lax.axis_size(axis))
    route = [(i - distance, i) for i in devices if i - distance in devices]
    return lax.ppermute(block, axis, route)


def rope_tables(positions, head_width):
    half_width = head_width // 2
    exponent = jnp.arange(half_width, dtype=jnp.float32) * (2.0 / head_width)
    frequency = rope_base ** (-exponent)
    angles = positions.astype(jnp.float32)[:, None] * frequency[None, :]
    cosine = jnp.concatenate([jnp.cos(angles), jnp.cos(angles)], axis=1)
    sine_table = jnp.concatenate([jnp.sin(angles), jnp.sin(angles)], axis=1)
    return (cosine, sine_table)


def rotate(signal, cosine, sine_table):
    half_width = signal.shape[-1] // 2
    turned = jnp.concatenate([-signal[:, half_width:], signal[:, :half_width]], axis=1)
    return signal * cosine + turned * sine_table


def rms_scale(signal, gain_vector):
    return (
        signal
        * lax.rsqrt(jnp.mean(signal * signal, axis=-1, keepdims=True) + epsilon)
        * gain_vector
    )


def layer(
    tokens, norm_gain, query_weight, keyval_weight, query_gain, key_gain, out_weight, post_gain
):
    tok_rows = tokens.shape[0]
    model_width = tokens.shape[1]
    head_width = query_weight.shape[1]
    col_share = post_gain.shape[0]
    n_zl = lax.axis_size("zl")
    n_x = lax.axis_size("x")
    n_core = lax.axis_size("core")
    ctx_index = lax.axis_index("ctx")
    core_index = lax.axis_index("core")
    tp_index = (lax.axis_index("zl") * n_x + lax.axis_index("x")) * n_core + core_index
    is_even = core_index == 0

    as_float = tokens.astype(jnp.float32)
    normed = rms_scale(as_float, norm_gain).astype(jnp.bfloat16)
    positions = ctx_index * tok_rows + jnp.arange(tok_rows, dtype=jnp.int32)
    cosine, sine_table = rope_tables(positions, head_width)

    projected = jnp.dot(normed, keyval_weight, preferred_element_type=jnp.float32)
    rotated = rotate(rms_scale(projected, key_gain), cosine, sine_table)
    own_block = jnp.where(is_even, rotated, projected).astype(jnp.bfloat16)
    n_tp = n_zl * n_x * n_core
    weight_block = lax.all_to_all(
        out_weight.reshape(head_width, n_tp, col_share), TP_AXES, 1, 0, tiled=True
    ).reshape(n_tp * head_width, col_share)
    span_count = WIN // tok_rows
    earlier = [from_behind(own_block, "ctx", offset) for offset in range(span_count, 0, -1)]
    own_window = jnp.concatenate(earlier + [own_block], axis=0)
    other_window = lax.ppermute(own_window, "core", [(0, 1), (1, 0)])
    weight_block, own_window, other_window = lax.optimization_barrier(
        (weight_block, own_window, other_window)
    )
    key_window = jnp.where(is_even, own_window, other_window)
    value_window = jnp.where(is_even, other_window, own_window)

    queries = jnp.dot(normed, query_weight, preferred_element_type=jnp.float32)
    queries = (
        rotate(rms_scale(queries, query_gain), cosine, sine_table) * query_scalar ** (-0.5)
    ).astype(jnp.bfloat16)

    key_pos = ctx_index * tok_rows - WIN + jnp.arange(WIN + tok_rows, dtype=jnp.int32)
    distance = positions[:, None] - key_pos[None, :]
    allowed = (key_pos[None, :] >= 0) & (distance >= 0) & (distance < WIN)
    scores = lax.dot_general(
        queries,
        key_window,
        (((1,), (1,)), ((), ())),
        preferred_element_type=jnp.float32,
    )
    scores = jnp.where(allowed, scores, -1e30)
    row_max = jnp.max(scores, axis=1, keepdims=True)
    lifted = jnp.exp(scores - row_max)
    weights = (lifted / jnp.sum(lifted, axis=1, keepdims=True)).astype(jnp.bfloat16)
    attended = jnp.dot(weights, value_window, preferred_element_type=jnp.float32).astype(
        jnp.bfloat16
    )

    all_heads = lax.all_gather(attended, TP_AXES, axis=1, tiled=True)
    summed = jnp.dot(all_heads, weight_block, preferred_element_type=jnp.float32)
    squares = jnp.sum(summed * summed, axis=1)
    for axis in ("core", "x", "zl"):
        squares = lax.psum(squares, axis)
    scaled = summed * lax.rsqrt(squares[:, None] / model_width + epsilon) * post_gain
    residual = lax.dynamic_slice_in_dim(tokens, tp_index * col_share, col_share, 1)
    return (residual.astype(jnp.float32) + scaled).astype(jnp.bfloat16)


def solution(mesh):
    n_ctx, n_tp = mesh.devices.shape
    n_core = 2
    n_x = 4
    n_zl = n_tp // (n_core * n_x)
    fine = Mesh(mesh.devices.reshape(n_ctx, n_zl, n_x, n_core), ("ctx",) + TP_AXES)
    return jax.shard_map(
        layer,
        mesh=fine,
        in_specs=(
            P("ctx", None),
            P(),
            P(None, TP_AXES),
            P(None, TP_AXES),
            P(),
            P(),
            P(TP_AXES, None),
            P(TP_AXES),
        ),
        out_specs=P("ctx", TP_AXES),
        check_vma=False,
    )
```

```python
import jax
import jax.numpy as jnp
from jax import lax
from jax.sharding import Mesh, PartitionSpec as P

WIN = 1024


epsilon = 1e-06
query_scalar = 168.0
rope_base = 10000.0

TP_AXES = ("zl", "x", "core")


def from_behind(block, axis, distance):
    devices = range(lax.axis_size(axis))
    route = [(i - distance, i) for i in devices if i - distance in devices]
    return lax.ppermute(block, axis, route)


def rope_tables(positions, head_width):
    half_width = head_width // 2
    exponent = jnp.arange(half_width, dtype=jnp.float32) * (2.0 / head_width)
    frequency = rope_base ** (-exponent)
    angles = positions.astype(jnp.float32)[:, None] * frequency[None, :]
    cosine = jnp.concatenate([jnp.cos(angles), jnp.cos(angles)], axis=1)
    sine_table = jnp.concatenate([jnp.sin(angles), jnp.sin(angles)], axis=1)
    return (cosine, sine_table)


def rotate(signal, cosine, sine_table):
    half_width = signal.shape[-1] // 2
    turned = jnp.concatenate([-signal[:, half_width:], signal[:, :half_width]], axis=1)
    return signal * cosine + turned * sine_table


def rms_scale(signal, gain_vector):
    return (
        signal
        * lax.rsqrt(jnp.mean(signal * signal, axis=-1, keepdims=True) + epsilon)
        * gain_vector
    )


def layer(
    tokens, norm_gain, query_weight, keyval_weight, query_gain, key_gain, out_weight, post_gain
):
    tok_rows = tokens.shape[0]
    model_width = tokens.shape[1]
    head_width = query_weight.shape[1]
    col_share = post_gain.shape[0]
    n_zl = lax.axis_size("zl")
    n_x = lax.axis_size("x")
    n_core = lax.axis_size("core")
    ctx_index = lax.axis_index("ctx")
    core_index = lax.axis_index("core")
    tp_index = (lax.axis_index("zl") * n_x + lax.axis_index("x")) * n_core + core_index
    is_even = core_index == 0

    as_float = tokens.astype(jnp.float32)
    normed = rms_scale(as_float, norm_gain).astype(jnp.bfloat16)
    positions = ctx_index * tok_rows + jnp.arange(tok_rows, dtype=jnp.int32)
    cosine, sine_table = rope_tables(positions, head_width)

    projected = jnp.dot(normed, keyval_weight, preferred_element_type=jnp.float32)
    rotated = rotate(rms_scale(projected, key_gain), cosine, sine_table)
    own_block = jnp.where(is_even, rotated, projected).astype(jnp.bfloat16)
    n_tp = n_zl * n_x * n_core
    weight_block = lax.all_to_all(
        out_weight.reshape(head_width, n_tp, col_share), TP_AXES, 1, 0, tiled=True
    ).reshape(n_tp * head_width, col_share)
    span_count = WIN // tok_rows
    earlier = [from_behind(own_block, "ctx", offset) for offset in range(span_count, 0, -1)]
    own_window = jnp.concatenate(earlier + [own_block], axis=0)
    other_window = lax.ppermute(own_window, "core", [(0, 1), (1, 0)])
    weight_block, own_window, other_window = lax.optimization_barrier(
        (weight_block, own_window, other_window)
    )
    key_window = jnp.where(is_even, own_window, other_window)
    value_window = jnp.where(is_even, other_window, own_window)

    queries = jnp.dot(normed, query_weight, preferred_element_type=jnp.float32)
    queries = (
        rotate(rms_scale(queries, query_gain), cosine, sine_table) * query_scalar ** (-0.5)
    ).astype(jnp.bfloat16)

    key_pos = ctx_index * tok_rows - WIN + jnp.arange(WIN + tok_rows, dtype=jnp.int32)
    distance = positions[:, None] - key_pos[None, :]
    allowed = (key_pos[None, :] >= 0) & (distance >= 0) & (distance < WIN)
    scores = lax.dot_general(
        queries,
        key_window,
        (((1,), (1,)), ((), ())),
        preferred_element_type=jnp.float32,
    )
    scores = jnp.where(allowed, scores, -1e30)
    row_max = jnp.max(scores, axis=1, keepdims=True)
    lifted = jnp.exp(scores - row_max)
    weights = (lifted / jnp.sum(lifted, axis=1, keepdims=True)).astype(jnp.bfloat16)
    attended = jnp.dot(weights, value_window, preferred_element_type=jnp.float32).astype(
        jnp.bfloat16
    )

    copies = jnp.broadcast_to(attended[None], (n_tp,) + attended.shape)
    all_heads = lax.all_to_all(copies, TP_AXES, 0, 0, tiled=True)
    summed = lax.dot_general(
        all_heads,
        weight_block.reshape(n_tp, head_width, col_share),
        (((0, 2), (0, 1)), ((), ())),
        preferred_element_type=jnp.float32,
    )
    squares = jnp.sum(summed * summed, axis=1)
    square_copies = jnp.broadcast_to(squares[None], (n_tp,) + squares.shape)
    squares = jnp.sum(lax.all_to_all(square_copies, TP_AXES, 0, 0, tiled=True), axis=0)
    scaled = summed * lax.rsqrt(squares[:, None] / model_width + epsilon) * post_gain
    residual = lax.dynamic_slice_in_dim(tokens, tp_index * col_share, col_share, 1)
    return (residual.astype(jnp.float32) + scaled).astype(jnp.bfloat16)


def solution(mesh):
    n_ctx, n_tp = mesh.devices.shape
    n_core = 2
    n_x = 4
    n_zl = n_tp // (n_core * n_x)
    fine = Mesh(mesh.devices.reshape(n_ctx, n_zl, n_x, n_core), ("ctx",) + TP_AXES)
    return jax.shard_map(
        layer,
        mesh=fine,
        in_specs=(
            P("ctx", None),
            P(),
            P(None, TP_AXES),
            P(None, TP_AXES),
            P(),
            P(),
            P(TP_AXES, None),
            P(TP_AXES),
        ),
        out_specs=P("ctx", TP_AXES),
        check_vma=False,
    )
```

```python
import jax
import jax.numpy as jnp
from jax import lax
from jax.sharding import Mesh, PartitionSpec as P

WIN = 1024


epsilon = 1e-06
query_scalar = 168.0
rope_base = 10000.0

TP_AXES = ("zl", "x", "core")
Z_HI = 4


def from_behind(block, axis, distance):
    devices = range(lax.axis_size(axis))
    route = [(i - distance, i) for i in devices if i - distance in devices]
    return lax.ppermute(block, axis, route)


def rope_tables(positions, head_width):
    half_width = head_width // 2
    exponent = jnp.arange(half_width, dtype=jnp.float32) * (2.0 / head_width)
    frequency = rope_base ** (-exponent)
    angles = positions.astype(jnp.float32)[:, None] * frequency[None, :]
    cosine = jnp.concatenate([jnp.cos(angles), jnp.cos(angles)], axis=1)
    sine_table = jnp.concatenate([jnp.sin(angles), jnp.sin(angles)], axis=1)
    return (cosine, sine_table)


def rotate(signal, cosine, sine_table):
    half_width = signal.shape[-1] // 2
    turned = jnp.concatenate([-signal[:, half_width:], signal[:, :half_width]], axis=1)
    return signal * cosine + turned * sine_table


def rms_scale(signal, gain_vector):
    return (
        signal
        * lax.rsqrt(jnp.mean(signal * signal, axis=-1, keepdims=True) + epsilon)
        * gain_vector
    )


def layer(
    tokens, norm_gain, query_weight, keyval_weight, query_gain, key_gain, out_weight, post_gain
):
    tok_rows = tokens.shape[0]
    model_width = tokens.shape[1]
    head_width = query_weight.shape[1]
    col_share = post_gain.shape[0]
    n_zl = lax.axis_size("zl")
    n_x = lax.axis_size("x")
    n_core = lax.axis_size("core")
    ctx_index = lax.axis_index("ctx")
    core_index = lax.axis_index("core")
    tp_index = (lax.axis_index("zl") * n_x + lax.axis_index("x")) * n_core + core_index
    is_even = core_index == 0

    as_float = tokens.astype(jnp.float32)
    normed = rms_scale(as_float, norm_gain).astype(jnp.bfloat16)
    positions = ctx_index * tok_rows + jnp.arange(tok_rows, dtype=jnp.int32)
    cosine, sine_table = rope_tables(positions, head_width)

    projected = jnp.dot(normed, keyval_weight, preferred_element_type=jnp.float32)
    rotated = rotate(rms_scale(projected, key_gain), cosine, sine_table)
    own_block = jnp.where(is_even, rotated, projected).astype(jnp.bfloat16)
    n_tp = n_zl * n_x * n_core
    weight_block = lax.all_to_all(
        out_weight.reshape(head_width, n_tp, col_share), TP_AXES, 1, 0, tiled=True
    ).reshape(n_tp * head_width, col_share)
    span_count = WIN // tok_rows
    n_ctx = lax.axis_size("ctx")
    devices = range(n_ctx)
    mid = [(c // Z_HI) * Z_HI + (c % Z_HI - 1) % Z_HI for c in devices]
    first_leg = [(c, mid[c]) for c in devices if c + span_count in devices]
    second_leg = [(mid[c], c + span_count) for c in devices if c + span_count in devices]
    far_block = lax.ppermute(lax.ppermute(own_block, "ctx", first_leg), "ctx", second_leg)
    earlier = [far_block] + [
        from_behind(own_block, "ctx", offset) for offset in range(span_count - 1, 0, -1)
    ]
    own_window = jnp.concatenate(earlier + [own_block], axis=0)
    other_window = lax.ppermute(own_window, "core", [(0, 1), (1, 0)])
    weight_block, own_window, other_window = lax.optimization_barrier(
        (weight_block, own_window, other_window)
    )
    key_window = jnp.where(is_even, own_window, other_window)
    value_window = jnp.where(is_even, other_window, own_window)

    queries = jnp.dot(normed, query_weight, preferred_element_type=jnp.float32)
    queries = (
        rotate(rms_scale(queries, query_gain), cosine, sine_table) * query_scalar ** (-0.5)
    ).astype(jnp.bfloat16)

    key_pos = ctx_index * tok_rows - WIN + jnp.arange(WIN + tok_rows, dtype=jnp.int32)
    distance = positions[:, None] - key_pos[None, :]
    allowed = (key_pos[None, :] >= 0) & (distance >= 0) & (distance < WIN)
    scores = lax.dot_general(
        queries,
        key_window,
        (((1,), (1,)), ((), ())),
        preferred_element_type=jnp.float32,
    )
    scores = jnp.where(allowed, scores, -1e30)
    row_max = jnp.max(scores, axis=1, keepdims=True)
    lifted = jnp.exp(scores - row_max)
    weights = (lifted / jnp.sum(lifted, axis=1, keepdims=True)).astype(jnp.bfloat16)
    attended = jnp.dot(weights, value_window, preferred_element_type=jnp.float32).astype(
        jnp.bfloat16
    )

    n_peer = n_zl * n_x
    copies = jnp.broadcast_to(attended[None], (n_peer,) + attended.shape)
    own_heads = lax.all_to_all(copies, ("zl", "x"), 0, 0, tiled=True)
    other_heads = lax.ppermute(own_heads, "core", [(0, 1), (1, 0)])
    rows = weight_block.reshape(n_peer, n_core, head_width, col_share)
    own_rows = jnp.where(is_even, rows[:, 0], rows[:, 1])
    other_rows = jnp.where(is_even, rows[:, 1], rows[:, 0])
    contract = (((0, 2), (0, 1)), ((), ()))
    summed = lax.dot_general(
        own_heads, own_rows, contract, preferred_element_type=jnp.float32
    ) + lax.dot_general(other_heads, other_rows, contract, preferred_element_type=jnp.float32)
    squares = jnp.sum(summed * summed, axis=1)
    square_copies = jnp.broadcast_to(squares[None], (n_tp,) + squares.shape)
    squares = jnp.sum(lax.all_to_all(square_copies, TP_AXES, 0, 0, tiled=True), axis=0)
    scaled = summed * lax.rsqrt(squares[:, None] / model_width + epsilon) * post_gain
    residual = lax.dynamic_slice_in_dim(tokens, tp_index * col_share, col_share, 1)
    return (residual.astype(jnp.float32) + scaled).astype(jnp.bfloat16)


def solution(mesh):
    n_ctx, n_tp = mesh.devices.shape
    n_core = 2
    n_x = 4
    n_zl = n_tp // (n_core * n_x)
    fine = Mesh(mesh.devices.reshape(n_ctx, n_zl, n_x, n_core), ("ctx",) + TP_AXES)
    return jax.shard_map(
        layer,
        mesh=fine,
        in_specs=(
            P("ctx", None),
            P(),
            P(None, TP_AXES),
            P(None, TP_AXES),
            P(),
            P(),
            P(TP_AXES, None),
            P(TP_AXES),
        ),
        out_specs=P("ctx", TP_AXES),
        check_vma=False,
    )
```

```python
import jax
import jax.numpy as jnp
from jax import lax
from jax.experimental import pallas as pl
from jax.sharding import Mesh, PartitionSpec as P

WIN = 1024


epsilon = 1e-06
query_scalar = 168.0
rope_base = 10000.0

TP_AXES = ("zl", "x", "core")


def from_behind(block, axis, distance):
    devices = range(lax.axis_size(axis))
    route = [(i - distance, i) for i in devices if i - distance in devices]
    return lax.ppermute(block, axis, route)


def rope_tables(positions, head_width):
    half_width = head_width // 2
    exponent = jnp.arange(half_width, dtype=jnp.float32) * (2.0 / head_width)
    frequency = rope_base ** (-exponent)
    angles = positions.astype(jnp.float32)[:, None] * frequency[None, :]
    cosine = jnp.concatenate([jnp.cos(angles), jnp.cos(angles)], axis=1)
    sine_table = jnp.concatenate([jnp.sin(angles), jnp.sin(angles)], axis=1)
    return (cosine, sine_table)


def rotate(signal, cosine, sine_table):
    half_width = signal.shape[-1] // 2
    turned = jnp.concatenate([-signal[:, half_width:], signal[:, :half_width]], axis=1)
    return signal * cosine + turned * sine_table


def rms_scale(signal, gain_vector):
    return (
        signal
        * lax.rsqrt(jnp.mean(signal * signal, axis=-1, keepdims=True) + epsilon)
        * gain_vector
    )


def norm_project_kernel(rows_ref, gain_ref, weight_ref, projected_ref, normed_ref):
    rows = rows_ref[...].astype(jnp.float32)
    scale = lax.rsqrt(jnp.mean(rows * rows, axis=-1, keepdims=True) + epsilon)
    normed = (rows * scale * gain_ref[...]).astype(jnp.bfloat16)
    normed_ref[...] = normed
    projected_ref[...] = jnp.dot(normed, weight_ref[...], preferred_element_type=jnp.float32)


def norm_project(tokens, norm_gain, weight, block_rows=128):
    tok_rows, model_width = tokens.shape
    width = weight.shape[1]
    return pl.pallas_call(
        norm_project_kernel,
        grid=(tok_rows // block_rows,),
        in_specs=[
            pl.BlockSpec((block_rows, model_width), lambda i: (i, 0)),
            pl.BlockSpec((1, model_width), lambda i: (0, 0)),
            pl.BlockSpec((model_width, width), lambda i: (0, 0)),
        ],
        out_specs=[
            pl.BlockSpec((block_rows, width), lambda i: (i, 0)),
            pl.BlockSpec((block_rows, model_width), lambda i: (i, 0)),
        ],
        out_shape=[
            jax.ShapeDtypeStruct((tok_rows, width), jnp.float32),
            jax.ShapeDtypeStruct((tok_rows, model_width), jnp.bfloat16),
        ],
    )(tokens, norm_gain.reshape(1, model_width), weight)


def layer(
    tokens, norm_gain, query_weight, keyval_weight, query_gain, key_gain, out_weight, post_gain
):
    tok_rows = tokens.shape[0]
    model_width = tokens.shape[1]
    head_width = query_weight.shape[1]
    col_share = post_gain.shape[0]
    n_zl = lax.axis_size("zl")
    n_x = lax.axis_size("x")
    n_core = lax.axis_size("core")
    ctx_index = lax.axis_index("ctx")
    core_index = lax.axis_index("core")
    tp_index = (lax.axis_index("zl") * n_x + lax.axis_index("x")) * n_core + core_index
    is_even = core_index == 0

    positions = ctx_index * tok_rows + jnp.arange(tok_rows, dtype=jnp.int32)
    cosine, sine_table = rope_tables(positions, head_width)

    projected, normed = norm_project(tokens, norm_gain, keyval_weight)
    rotated = rotate(rms_scale(projected, key_gain), cosine, sine_table)
    own_block = jnp.where(is_even, rotated, projected).astype(jnp.bfloat16)
    n_tp = n_zl * n_x * n_core
    weight_block = lax.all_to_all(
        out_weight.reshape(head_width, n_tp, col_share), TP_AXES, 1, 0, tiled=True
    ).reshape(n_tp * head_width, col_share)
    span_count = WIN // tok_rows
    earlier = [from_behind(own_block, "ctx", offset) for offset in range(span_count, 0, -1)]
    own_window = jnp.concatenate(earlier + [own_block], axis=0)
    other_window = lax.ppermute(own_window, "core", [(0, 1), (1, 0)])
    weight_block, own_window, other_window = lax.optimization_barrier(
        (weight_block, own_window, other_window)
    )
    key_window = jnp.where(is_even, own_window, other_window)
    value_window = jnp.where(is_even, other_window, own_window)

    queries = jnp.dot(normed, query_weight, preferred_element_type=jnp.float32)
    queries = (
        rotate(rms_scale(queries, query_gain), cosine, sine_table) * query_scalar ** (-0.5)
    ).astype(jnp.bfloat16)

    key_pos = ctx_index * tok_rows - WIN + jnp.arange(WIN + tok_rows, dtype=jnp.int32)
    distance = positions[:, None] - key_pos[None, :]
    allowed = (key_pos[None, :] >= 0) & (distance >= 0) & (distance < WIN)
    scores = lax.dot_general(
        queries,
        key_window,
        (((1,), (1,)), ((), ())),
        preferred_element_type=jnp.float32,
    )
    scores = jnp.where(allowed, scores, -1e30)
    row_max = jnp.max(scores, axis=1, keepdims=True)
    lifted = jnp.exp(scores - row_max)
    weights = (lifted / jnp.sum(lifted, axis=1, keepdims=True)).astype(jnp.bfloat16)
    attended = jnp.dot(weights, value_window, preferred_element_type=jnp.float32).astype(
        jnp.bfloat16
    )

    n_peer = n_zl * n_x
    copies = jnp.broadcast_to(attended[None], (n_peer,) + attended.shape)
    own_heads = lax.all_to_all(copies, ("zl", "x"), 0, 0, tiled=True)
    other_heads = lax.ppermute(own_heads, "core", [(0, 1), (1, 0)])
    rows = weight_block.reshape(n_peer, n_core, head_width, col_share)
    own_rows = jnp.where(is_even, rows[:, 0], rows[:, 1])
    other_rows = jnp.where(is_even, rows[:, 1], rows[:, 0])
    contract = (((0, 2), (0, 1)), ((), ()))
    summed = lax.dot_general(
        own_heads, own_rows, contract, preferred_element_type=jnp.float32
    ) + lax.dot_general(other_heads, other_rows, contract, preferred_element_type=jnp.float32)
    squares = jnp.sum(summed * summed, axis=1)
    square_copies = jnp.broadcast_to(squares[None], (n_tp,) + squares.shape)
    squares = jnp.sum(lax.all_to_all(square_copies, TP_AXES, 0, 0, tiled=True), axis=0)
    scaled = summed * lax.rsqrt(squares[:, None] / model_width + epsilon) * post_gain
    residual = lax.dynamic_slice_in_dim(tokens, tp_index * col_share, col_share, 1)
    return (residual.astype(jnp.float32) + scaled).astype(jnp.bfloat16)


def solution(mesh):
    n_ctx, n_tp = mesh.devices.shape
    n_core = 2
    n_x = 4
    n_zl = n_tp // (n_core * n_x)
    fine = Mesh(mesh.devices.reshape(n_ctx, n_zl, n_x, n_core), ("ctx",) + TP_AXES)
    return jax.shard_map(
        layer,
        mesh=fine,
        in_specs=(
            P("ctx", None),
            P(),
            P(None, TP_AXES),
            P(None, TP_AXES),
            P(),
            P(),
            P(TP_AXES, None),
            P(TP_AXES),
        ),
        out_specs=P("ctx", TP_AXES),
        check_vma=False,
    )
```

```python
import jax
import jax.numpy as jnp
from jax import lax
from jax.experimental import pallas as pl
from jax.sharding import Mesh, PartitionSpec as P

WIN = 1024


epsilon = 1e-06
query_scalar = 168.0
rope_base = 10000.0

TP_AXES = ("zl", "x", "core")


def from_behind(block, axis, distance):
    devices = range(lax.axis_size(axis))
    route = [(i - distance, i) for i in devices if i - distance in devices]
    return lax.ppermute(block, axis, route)


def rope_tables(positions, head_width):
    half_width = head_width // 2
    exponent = jnp.arange(half_width, dtype=jnp.float32) * (2.0 / head_width)
    frequency = rope_base ** (-exponent)
    angles = positions.astype(jnp.float32)[:, None] * frequency[None, :]
    cosine = jnp.concatenate([jnp.cos(angles), jnp.cos(angles)], axis=1)
    sine_table = jnp.concatenate([jnp.sin(angles), jnp.sin(angles)], axis=1)
    return (cosine, sine_table)


def rotate(signal, cosine, sine_table):
    half_width = signal.shape[-1] // 2
    turned = jnp.concatenate([-signal[:, half_width:], signal[:, :half_width]], axis=1)
    return signal * cosine + turned * sine_table


def rms_scale(signal, gain_vector):
    return (
        signal
        * lax.rsqrt(jnp.mean(signal * signal, axis=-1, keepdims=True) + epsilon)
        * gain_vector
    )


def norm_project_kernel(rows_ref, gain_ref, weight_ref, projected_ref, scale_ref):
    rows = rows_ref[...].astype(jnp.float32)
    scale = lax.rsqrt(jnp.mean(rows * rows, axis=-1, keepdims=True) + epsilon)
    scale_ref[...] = scale
    normed = (rows * scale * gain_ref[...]).astype(jnp.bfloat16)
    projected_ref[...] = jnp.dot(normed, weight_ref[...], preferred_element_type=jnp.float32)


def norm_project(tokens, norm_gain, weight, block_rows=128):
    tok_rows, model_width = tokens.shape
    width = weight.shape[1]
    return pl.pallas_call(
        norm_project_kernel,
        grid=(tok_rows // block_rows,),
        in_specs=[
            pl.BlockSpec((block_rows, model_width), lambda i: (i, 0)),
            pl.BlockSpec((1, model_width), lambda i: (0, 0)),
            pl.BlockSpec((model_width, width), lambda i: (0, 0)),
        ],
        out_specs=[
            pl.BlockSpec((block_rows, width), lambda i: (i, 0)),
            pl.BlockSpec((block_rows, 1), lambda i: (i, 0)),
        ],
        out_shape=[
            jax.ShapeDtypeStruct((tok_rows, width), jnp.float32),
            jax.ShapeDtypeStruct((tok_rows, 1), jnp.float32),
        ],
    )(tokens, norm_gain.reshape(1, model_width), weight)


def layer(
    tokens, norm_gain, query_weight, keyval_weight, query_gain, key_gain, out_weight, post_gain
):
    tok_rows = tokens.shape[0]
    model_width = tokens.shape[1]
    head_width = query_weight.shape[1]
    col_share = post_gain.shape[0]
    n_zl = lax.axis_size("zl")
    n_x = lax.axis_size("x")
    n_core = lax.axis_size("core")
    ctx_index = lax.axis_index("ctx")
    core_index = lax.axis_index("core")
    tp_index = (lax.axis_index("zl") * n_x + lax.axis_index("x")) * n_core + core_index
    is_even = core_index == 0

    positions = ctx_index * tok_rows + jnp.arange(tok_rows, dtype=jnp.int32)
    cosine, sine_table = rope_tables(positions, head_width)

    projected, row_scale = norm_project(tokens, norm_gain, keyval_weight)
    rotated = rotate(rms_scale(projected, key_gain), cosine, sine_table)
    own_block = jnp.where(is_even, rotated, projected).astype(jnp.bfloat16)
    n_tp = n_zl * n_x * n_core
    weight_block = lax.all_to_all(
        out_weight.reshape(head_width, n_tp, col_share), TP_AXES, 1, 0, tiled=True
    ).reshape(n_tp * head_width, col_share)
    span_count = WIN // tok_rows
    earlier = [from_behind(own_block, "ctx", offset) for offset in range(span_count, 0, -1)]
    own_window = jnp.concatenate(earlier + [own_block], axis=0)
    other_window = lax.ppermute(own_window, "core", [(0, 1), (1, 0)])
    weight_block, own_window, other_window = lax.optimization_barrier(
        (weight_block, own_window, other_window)
    )
    key_window = jnp.where(is_even, own_window, other_window)
    value_window = jnp.where(is_even, other_window, own_window)

    normed = (tokens.astype(jnp.float32) * row_scale * norm_gain).astype(jnp.bfloat16)
    queries = jnp.dot(normed, query_weight, preferred_element_type=jnp.float32)
    queries = (
        rotate(rms_scale(queries, query_gain), cosine, sine_table) * query_scalar ** (-0.5)
    ).astype(jnp.bfloat16)

    key_pos = ctx_index * tok_rows - WIN + jnp.arange(WIN + tok_rows, dtype=jnp.int32)
    distance = positions[:, None] - key_pos[None, :]
    allowed = (key_pos[None, :] >= 0) & (distance >= 0) & (distance < WIN)
    scores = lax.dot_general(
        queries,
        key_window,
        (((1,), (1,)), ((), ())),
        preferred_element_type=jnp.float32,
    )
    scores = jnp.where(allowed, scores, -1e30)
    row_max = jnp.max(scores, axis=1, keepdims=True)
    lifted = jnp.exp(scores - row_max)
    weights = (lifted / jnp.sum(lifted, axis=1, keepdims=True)).astype(jnp.bfloat16)
    attended = jnp.dot(weights, value_window, preferred_element_type=jnp.float32).astype(
        jnp.bfloat16
    )

    n_peer = n_zl * n_x
    copies = jnp.broadcast_to(attended[None], (n_peer,) + attended.shape)
    own_heads = lax.all_to_all(copies, ("zl", "x"), 0, 0, tiled=True)
    other_heads = lax.ppermute(own_heads, "core", [(0, 1), (1, 0)])
    rows = weight_block.reshape(n_peer, n_core, head_width, col_share)
    own_rows = jnp.where(is_even, rows[:, 0], rows[:, 1])
    other_rows = jnp.where(is_even, rows[:, 1], rows[:, 0])
    contract = (((0, 2), (0, 1)), ((), ()))
    summed = lax.dot_general(
        own_heads, own_rows, contract, preferred_element_type=jnp.float32
    ) + lax.dot_general(other_heads, other_rows, contract, preferred_element_type=jnp.float32)
    squares = jnp.sum(summed * summed, axis=1)
    square_copies = jnp.broadcast_to(squares[None], (n_tp,) + squares.shape)
    squares = jnp.sum(lax.all_to_all(square_copies, TP_AXES, 0, 0, tiled=True), axis=0)
    scaled = summed * lax.rsqrt(squares[:, None] / model_width + epsilon) * post_gain
    residual = lax.dynamic_slice_in_dim(tokens, tp_index * col_share, col_share, 1)
    return (residual.astype(jnp.float32) + scaled).astype(jnp.bfloat16)


def solution(mesh):
    n_ctx, n_tp = mesh.devices.shape
    n_core = 2
    n_x = 4
    n_zl = n_tp // (n_core * n_x)
    fine = Mesh(mesh.devices.reshape(n_ctx, n_zl, n_x, n_core), ("ctx",) + TP_AXES)
    return jax.shard_map(
        layer,
        mesh=fine,
        in_specs=(
            P("ctx", None),
            P(),
            P(None, TP_AXES),
            P(None, TP_AXES),
            P(),
            P(),
            P(TP_AXES, None),
            P(TP_AXES),
        ),
        out_specs=P("ctx", TP_AXES),
        check_vma=False,
    )
```

```python
import jax
import jax.numpy as jnp
from jax import lax
from jax.sharding import Mesh, PartitionSpec as P


WIN = 1024


epsilon = 1e-06
query_scalar = 168.0
rope_base = 10000.0

TP_AXES = ("zl", "x", "core")


def from_behind(block, axis, distance):
    devices = range(lax.axis_size(axis))
    route = [(i - distance, i) for i in devices if i - distance in devices]
    return lax.ppermute(block, axis, route)


def rope_tables(positions, head_width):
    half_width = head_width // 2
    exponent = jnp.arange(half_width, dtype=jnp.float32) * (2.0 / head_width)
    frequency = rope_base ** (-exponent)
    angles = positions.astype(jnp.float32)[:, None] * frequency[None, :]
    cosine = jnp.concatenate([jnp.cos(angles), jnp.cos(angles)], axis=1)
    sine_table = jnp.concatenate([jnp.sin(angles), jnp.sin(angles)], axis=1)
    return (cosine, sine_table)


def rotate(signal, cosine, sine_table):
    half_width = signal.shape[-1] // 2
    turned = jnp.concatenate([-signal[:, half_width:], signal[:, :half_width]], axis=1)
    return signal * cosine + turned * sine_table


def rms_scale(signal, gain_vector):
    return (
        signal
        * lax.rsqrt(jnp.mean(signal * signal, axis=-1, keepdims=True) + epsilon)
        * gain_vector
    )


def layer(
    tokens, norm_gain, query_weight, keyval_weight, query_gain, key_gain, out_weight, post_gain
):
    tok_rows = tokens.shape[0]
    model_width = tokens.shape[1]
    head_width = query_weight.shape[1]
    col_share = post_gain.shape[0]
    n_zl = lax.axis_size("zl")
    n_x = lax.axis_size("x")
    n_core = lax.axis_size("core")
    ctx_index = lax.axis_index("ctx")
    core_index = lax.axis_index("core")
    tp_index = (lax.axis_index("zl") * n_x + lax.axis_index("x")) * n_core + core_index
    is_even = core_index == 0

    as_float = tokens.astype(jnp.float32)
    normed = rms_scale(as_float, norm_gain).astype(jnp.bfloat16)
    positions = ctx_index * tok_rows + jnp.arange(tok_rows, dtype=jnp.int32)
    cosine, sine_table = rope_tables(positions, head_width)

    projected = jnp.dot(normed, keyval_weight, preferred_element_type=jnp.float32)
    rotated = rotate(rms_scale(projected, key_gain), cosine, sine_table)
    own_block = jnp.where(is_even, rotated, projected).astype(jnp.bfloat16)
    n_tp = n_zl * n_x * n_core
    weight_block = lax.all_to_all(
        out_weight.reshape(head_width, n_tp, col_share), TP_AXES, 1, 0, tiled=True
    ).reshape(n_tp * head_width, col_share)
    span_count = WIN // tok_rows
    earlier = [from_behind(own_block, "ctx", offset) for offset in range(span_count, 0, -1)]
    own_window = jnp.concatenate(earlier + [own_block], axis=0)
    other_window = lax.ppermute(own_window, "core", [(0, 1), (1, 0)])
    weight_block, own_window, other_window = lax.optimization_barrier(
        (weight_block, own_window, other_window)
    )
    key_window = jnp.where(is_even, own_window, other_window)
    value_window = jnp.where(is_even, other_window, own_window)

    queries = jnp.dot(normed, query_weight, preferred_element_type=jnp.float32)
    queries = (
        rotate(rms_scale(queries, query_gain), cosine, sine_table) * query_scalar ** (-0.5)
    ).astype(jnp.bfloat16)

    key_pos = ctx_index * tok_rows - WIN + jnp.arange(WIN + tok_rows, dtype=jnp.int32)
    distance = positions[:, None] - key_pos[None, :]
    allowed = (key_pos[None, :] >= 0) & (distance >= 0) & (distance < WIN)
    scores = lax.dot_general(
        queries,
        key_window,
        (((1,), (1,)), ((), ())),
        preferred_element_type=jnp.float32,
    )
    scores = jnp.where(allowed, scores, -1e30)
    row_max = jnp.max(scores, axis=1, keepdims=True)
    lifted = jnp.exp(scores - row_max)
    weights = (lifted / jnp.sum(lifted, axis=1, keepdims=True)).astype(jnp.bfloat16)
    attended = jnp.dot(weights, value_window, preferred_element_type=jnp.float32).astype(
        jnp.bfloat16
    )

    n_peer = n_zl * n_x
    copies = jnp.broadcast_to(attended[None], (n_peer,) + attended.shape)
    own_heads = lax.all_to_all(copies, ("zl", "x"), 0, 0, tiled=True)
    other_heads = lax.ppermute(own_heads, "core", [(0, 1), (1, 0)])
    rows = weight_block.reshape(n_peer, n_core, head_width, col_share)
    own_rows = jnp.where(is_even, rows[:, 0], rows[:, 1])
    other_rows = jnp.where(is_even, rows[:, 1], rows[:, 0])
    contract = (((0, 2), (0, 1)), ((), ()))
    summed = lax.dot_general(
        own_heads, own_rows, contract, preferred_element_type=jnp.float32
    ) + lax.dot_general(other_heads, other_rows, contract, preferred_element_type=jnp.float32)
    squares = jnp.sum(summed * summed, axis=1)
    square_copies = jnp.broadcast_to(squares[None], (n_tp,) + squares.shape)
    squares = jnp.sum(lax.all_to_all(square_copies, TP_AXES, 0, 0, tiled=True), axis=0)
    scaled = summed * lax.rsqrt(squares[:, None] / model_width + epsilon) * post_gain
    residual = lax.dynamic_slice_in_dim(tokens, tp_index * col_share, col_share, 1)
    return (residual.astype(jnp.float32) + scaled).astype(jnp.bfloat16)


def solution(mesh):
    n_ctx, n_tp = mesh.devices.shape
    n_core = 2
    n_x = 4
    n_zl = n_tp // (n_core * n_x)
    fine = Mesh(mesh.devices.reshape(n_ctx, n_zl, n_x, n_core), ("ctx",) + TP_AXES)
    return jax.shard_map(
        layer,
        mesh=fine,
        in_specs=(
            P("ctx", None),
            P(),
            P(None, TP_AXES),
            P(None, TP_AXES),
            P(),
            P(),
            P(TP_AXES, None),
            P(TP_AXES),
        ),
        out_specs=P("ctx", TP_AXES),
        check_vma=False,
    )
```

```python
import jax
import jax.numpy as jnp
from jax import lax
from jax.sharding import Mesh, PartitionSpec as P


WIN = 1024


epsilon = 1e-06
query_scalar = 168.0
rope_base = 10000.0

TP_AXES = ("zl", "x", "core")


def from_behind(block, axis, distance):
    devices = range(lax.axis_size(axis))
    route = [(i - distance, i) for i in devices if i - distance in devices]
    return lax.ppermute(block, axis, route)


def rope_tables(positions, head_width):
    half_width = head_width // 2
    exponent = jnp.arange(half_width, dtype=jnp.float32) * (2.0 / head_width)
    frequency = rope_base ** (-exponent)
    angles = positions.astype(jnp.float32)[:, None] * frequency[None, :]
    cosine = jnp.concatenate([jnp.cos(angles), jnp.cos(angles)], axis=1)
    sine_table = jnp.concatenate([jnp.sin(angles), jnp.sin(angles)], axis=1)
    return (cosine, sine_table)


def rotate(signal, cosine, sine_table):
    half_width = signal.shape[-1] // 2
    turned = jnp.concatenate([-signal[:, half_width:], signal[:, :half_width]], axis=1)
    return signal * cosine + turned * sine_table


def rms_scale(signal, gain_vector):
    return (
        signal
        * lax.rsqrt(jnp.mean(signal * signal, axis=-1, keepdims=True) + epsilon)
        * gain_vector
    )


def layer(
    tokens, norm_gain, query_weight, keyval_weight, query_gain, key_gain, out_weight, post_gain
):
    tok_rows = tokens.shape[0]
    model_width = tokens.shape[1]
    head_width = query_weight.shape[1]
    col_share = post_gain.shape[0]
    n_zl = lax.axis_size("zl")
    n_x = lax.axis_size("x")
    n_core = lax.axis_size("core")
    ctx_index = lax.axis_index("ctx")
    core_index = lax.axis_index("core")
    tp_index = (lax.axis_index("zl") * n_x + lax.axis_index("x")) * n_core + core_index
    is_even = core_index == 0

    as_float = tokens.astype(jnp.float32)
    normed = rms_scale(as_float, norm_gain).astype(jnp.bfloat16)
    positions = ctx_index * tok_rows + jnp.arange(tok_rows, dtype=jnp.int32)
    cosine, sine_table = rope_tables(positions, head_width)

    both = jnp.dot(
        normed,
        jnp.concatenate([keyval_weight, query_weight], axis=1),
        preferred_element_type=jnp.float32,
    )
    projected = both[:, :head_width]
    rotated = rotate(rms_scale(projected, key_gain), cosine, sine_table)
    own_block = jnp.where(is_even, rotated, projected).astype(jnp.bfloat16)
    n_tp = n_zl * n_x * n_core
    weight_block = lax.all_to_all(
        out_weight.reshape(head_width, n_tp, col_share), TP_AXES, 1, 0, tiled=True
    ).reshape(n_tp * head_width, col_share)
    span_count = WIN // tok_rows
    earlier = [from_behind(own_block, "ctx", offset) for offset in range(span_count, 0, -1)]
    own_window = jnp.concatenate(earlier + [own_block], axis=0)
    other_window = lax.ppermute(own_window, "core", [(0, 1), (1, 0)])
    weight_block, own_window, other_window = lax.optimization_barrier(
        (weight_block, own_window, other_window)
    )
    key_window = jnp.where(is_even, own_window, other_window)
    value_window = jnp.where(is_even, other_window, own_window)

    queries = both[:, head_width:]
    queries = (
        rotate(rms_scale(queries, query_gain), cosine, sine_table) * query_scalar ** (-0.5)
    ).astype(jnp.bfloat16)

    key_pos = ctx_index * tok_rows - WIN + jnp.arange(WIN + tok_rows, dtype=jnp.int32)
    distance = positions[:, None] - key_pos[None, :]
    allowed = (key_pos[None, :] >= 0) & (distance >= 0) & (distance < WIN)
    scores = lax.dot_general(
        queries,
        key_window,
        (((1,), (1,)), ((), ())),
        preferred_element_type=jnp.float32,
    )
    scores = jnp.where(allowed, scores, -1e30)
    row_max = jnp.max(scores, axis=1, keepdims=True)
    lifted = jnp.exp(scores - row_max)
    weights = (lifted / jnp.sum(lifted, axis=1, keepdims=True)).astype(jnp.bfloat16)
    attended = jnp.dot(weights, value_window, preferred_element_type=jnp.float32).astype(
        jnp.bfloat16
    )

    n_peer = n_zl * n_x
    copies = jnp.broadcast_to(attended[None], (n_peer,) + attended.shape)
    own_heads = lax.all_to_all(copies, ("zl", "x"), 0, 0, tiled=True)
    other_heads = lax.ppermute(own_heads, "core", [(0, 1), (1, 0)])
    rows = weight_block.reshape(n_peer, n_core, head_width, col_share)
    own_rows = jnp.where(is_even, rows[:, 0], rows[:, 1])
    other_rows = jnp.where(is_even, rows[:, 1], rows[:, 0])
    contract = (((0, 2), (0, 1)), ((), ()))
    summed = lax.dot_general(
        own_heads, own_rows, contract, preferred_element_type=jnp.float32
    ) + lax.dot_general(other_heads, other_rows, contract, preferred_element_type=jnp.float32)
    squares = jnp.sum(summed * summed, axis=1)
    square_copies = jnp.broadcast_to(squares[None], (n_tp,) + squares.shape)
    squares = jnp.sum(lax.all_to_all(square_copies, TP_AXES, 0, 0, tiled=True), axis=0)
    scaled = summed * lax.rsqrt(squares[:, None] / model_width + epsilon) * post_gain
    residual = lax.dynamic_slice_in_dim(tokens, tp_index * col_share, col_share, 1)
    return (residual.astype(jnp.float32) + scaled).astype(jnp.bfloat16)


def solution(mesh):
    n_ctx, n_tp = mesh.devices.shape
    n_core = 2
    n_x = 4
    n_zl = n_tp // (n_core * n_x)
    fine = Mesh(mesh.devices.reshape(n_ctx, n_zl, n_x, n_core), ("ctx",) + TP_AXES)
    return jax.shard_map(
        layer,
        mesh=fine,
        in_specs=(
            P("ctx", None),
            P(),
            P(None, TP_AXES),
            P(None, TP_AXES),
            P(),
            P(),
            P(TP_AXES, None),
            P(TP_AXES),
        ),
        out_specs=P("ctx", TP_AXES),
        check_vma=False,
    )
```
